256 devices in a mesh: dp: 64 (over x, z, core), tensor: 4 (over y).
Axes of the slice: x: 4, y: 4, z: 8, core: 2. Of those that a mesh axis runs over, the one named last changes fastest.
Arguments:
- tokens: bfloat16 [512, 16384], P('dp', 'tensor'), may hold values from -6 to 6
- clip_act: float32 [16384], P('tensor'), may hold values from 0.5 to 4
- weight: bfloat16 [16384, 49152], P('tensor', 'dp'), may hold values from -0.046875 to 0.046875
- clip_weight: float32 [49152], P('dp'), may hold values from 0.003 to 0.03
- cotangent: bfloat16 [512, 49152], P('tensor', 'dp'), may hold values from -16 to 16
Outputs:
- projected: bfloat16 [512, 49152], P('tensor', 'dp')
- token_grad: bfloat16 [512, 16384], P('dp', 'tensor')
- weight_grad: bfloat16 [16384, 49152], P('tensor', 'dp')
- clip_act_grad: float32 [16384], P('tensor')
- clip_weight_grad: float32 [49152], P('dp')
The draws below stay inside these ranges and needn't reach their ends.
All inputs are finite; a program needn't handle non-finite values.
Results may differ from the reference program's by a relative error of at most 0.009.
Values may be sent and summed in bfloat16 or wider, within the bound.
No kernel may reach another device: no remote copies, remote signals or barrier semaphores. Data moves between devices by JAX's collectives and lax.ppermute only.
A program may use at most 128 MiB of HBM per device.

```python
import math
import jax
import jax.numpy as jnp
from jax import lax

D = 16384
FF = 49152
TOKENS = 512


def with_spikes(drawn, stream_key, source, target, parts, factor):
    owner, partner = [(jnp.arange(drawn.shape[dim]) // (drawn.shape[dim] // parts)).reshape([-1 if axis == dim else 1 for axis in range(drawn.ndim)]) for dim in (source, target)]
    chosen = jax.random.permutation(stream_key, parts)[partner]
    strong = (owner == chosen) | (owner == (partner + parts // 2) % parts)
    return jnp.where(strong, factor * drawn, drawn)


def block_levels(key, dims, split, smallest, largest):
    factor_of = 1.0
    for position, blocks in split:
        steps = jax.random.uniform(jax.random.fold_in(jax.random.fold_in(key, 6), position), (blocks,), jnp.float32, smallest / len(split), largest / len(split))
        factor_of = factor_of * jnp.repeat(jnp.exp(steps), dims[position] // blocks).reshape((-1,) + (1,) * (len(dims) - 1 - position))
    return factor_of


def bell_draw(key, extent, spread, limit, cuts=(), kind=jnp.bfloat16):
    entries = spread * jax.random.normal(key, extent, jnp.float32)
    if cuts:
        entries = entries * block_levels(key, extent, cuts, -0.22, 0.18)
    return jnp.clip(entries, -limit, limit).astype(kind)


def bell_draw_with(key, shape, deviation, limit, split, heavy, kind=jnp.bfloat16):
    drawn = deviation * jax.random.normal(key, shape, jnp.float32)
    if split:
        drawn = drawn * block_levels(key, shape, split, -0.22, 0.18)
    return jnp.clip(with_spikes(drawn, jax.random.fold_in(key, 3), *heavy), -limit, limit).astype(kind)


def setup_inputs(seed: int = 0) -> dict:
    splits = jax.random.split(jax.random.key(seed), 6)
    return {
        "tokens": bell_draw(splits[0], (TOKENS, D), 1.0, 6.0, ((0, 64), (1, 4))),
        "clip_act": jnp.clip(jnp.exp(math.log(4.0) - 2.0794415 * jax.random.uniform(splits[1], (D,), jnp.float32) ** block_levels(splits[1], (D,), ((0, 4),), -0.2, 0.2)), 0.5, 4.0),
        "weight": bell_draw(splits[2], (D, FF), D ** -0.5, 0.046875, ((0, 4), (1, 64))),
        "clip_weight": jnp.clip(jnp.exp(math.log(0.03) - 2.3025851 * jax.random.uniform(splits[3], (FF,), jnp.float32) ** block_levels(splits[3], (FF,), ((0, 64),), -0.2, 0.2)), 0.003, 0.03),
        "cotangent": bell_draw_with(splits[4], (TOKENS, FF), 1.0, 16.0, ((0, 4), (1, 64)), (1, 0, 64, 4.0)),
    }


def sylvester(order):
    index = lax.iota(jnp.int32, order)
    joined = jnp.bitwise_and(index[:, None], index[None, :])
    parity = jnp.zeros((order, order), jnp.int32)
    for bit_number in range(max(order.bit_length() - 1, 0)):
        parity = parity + jnp.bitwise_and(jnp.right_shift(joined, bit_number), 1)
    return (1 - 2 * jnp.bitwise_and(parity, 1)).astype(jnp.float32)

def rotate_full(values):
    row_total, width = values.shape
    levels = width.bit_length() - 1
    outer = 2 ** (levels // 2)
    inner = width // outer
    blocks = values.reshape(row_total, outer, inner)
    blocks = jnp.einsum('rab,ac->rcb', blocks, sylvester(outer), precision=lax.Precision.HIGHEST)
    blocks = jnp.einsum('rcb,bd->rcd', blocks, sylvester(inner), precision=lax.Precision.HIGHEST)
    return blocks.reshape(row_total, width) * (1.0 / math.sqrt(width))

def reference(tokens, clip_act, weight, clip_weight, cotangent):
    rotated = rotate_full(tokens.astype(jnp.float32))
    ratio_act = rotated / clip_act
    tanh_act = jnp.tanh(ratio_act)
    quant_act = (clip_act * tanh_act).astype(jnp.bfloat16)
    slope_act = 1.0 - tanh_act * tanh_act
    edge_act = tanh_act - ratio_act * slope_act
    row_total, width = tokens.shape
    hidden = weight.shape[1]
    block_cols = math.gcd(hidden, 1024)
    block_count = hidden // block_cols

    def one_block(carry, block_index):
        first_col = block_index * block_cols
        weight_block = lax.dynamic_slice_in_dim(weight, first_col, block_cols, 1)
        clip_block = lax.dynamic_slice_in_dim(clip_weight, first_col, block_cols, 0)
        grad_block = lax.dynamic_slice_in_dim(cotangent, first_col, block_cols, 1)
        ratio_weight = weight_block.astype(jnp.float32) / clip_block
        tanh_weight = jnp.tanh(ratio_weight)
        quant_weight = (clip_block * tanh_weight).astype(jnp.bfloat16)
        outputs = jnp.dot(quant_act, quant_weight, preferred_element_type=jnp.float32).astype(jnp.bfloat16)
        carry = carry + jnp.dot(grad_block, quant_weight.T, preferred_element_type=jnp.float32)
        weight_prod = jnp.dot(quant_act.T, grad_block, preferred_element_type=jnp.float32)
        slope_weight = 1.0 - tanh_weight * tanh_weight
        weight_grad = (weight_prod * slope_weight).astype(jnp.bfloat16)
        clip_grad = lax.optimization_barrier(jnp.sum(weight_prod * (tanh_weight - ratio_weight * slope_weight), axis=0))
        return (carry, (outputs, weight_grad, clip_grad))
    initial = jnp.zeros((row_total, width), jnp.float32)
    act_prod, stacked = lax.scan(one_block, initial, jnp.arange(block_count, dtype=jnp.int32))
    outputs, weight_grads, clip_grads = stacked
    projected = jnp.transpose(outputs, (1, 0, 2)).reshape(row_total, hidden)
    weight_grad = jnp.transpose(weight_grads, (1, 0, 2)).reshape(width, hidden)
    clip_weight_grad = clip_grads.reshape(hidden)
    clip_act_grad = lax.optimization_barrier(jnp.sum(act_prod * edge_act, axis=0))
    token_grad = rotate_full(act_prod * slope_act).astype(jnp.bfloat16)
    return (projected, token_grad, weight_grad, clip_act_grad, clip_weight_grad)
```

```python
import math

import jax
import jax.numpy as jnp
from jax import lax
from jax.sharding import PartitionSpec as P


def swapped(block, axis, bit):
    count = lax.axis_size(axis)
    route = []
    for low in range(count):
        high = low | 1 << bit
        if high != low and high < count:
            route += [(low, high), (high, low)]
    return lax.ppermute(block, axis, route)


def sylvester(order):
    index = lax.iota(jnp.int32, order)
    joined = jnp.bitwise_and(index[:, None], index[None, :])
    parity = jnp.zeros((order, order), jnp.int32)
    for bit_number in range(max(order.bit_length() - 1, 0)):
        parity = parity + jnp.bitwise_and(jnp.right_shift(joined, bit_number), 1)
    return (1 - 2 * jnp.bitwise_and(parity, 1)).astype(jnp.float32)


def local_rotate(values, norm_factor):
    row_total, width = values.shape
    levels = width.bit_length() - 1
    outer = 2 ** (levels // 2)
    inner = width // outer
    blocks = values.reshape(row_total, outer, inner)
    blocks = jnp.einsum("rab,ac->rcb", blocks, sylvester(outer), precision=lax.Precision.HIGHEST)
    blocks = jnp.einsum("rcb,bd->rcd", blocks, sylvester(inner), precision=lax.Precision.HIGHEST)
    return blocks.reshape(row_total, width) * norm_factor


def rotate(values):
    group_size = lax.axis_size("tensor")
    norm_factor = 1.0 / math.sqrt(values.shape[1] * group_size)
    mixed = local_rotate(values, norm_factor)
    position = lax.axis_index("tensor")
    for bit_number in range(group_size.bit_length() - 1):
        partner = swapped(mixed, "tensor", bit_number)
        upper = jnp.bitwise_and(jnp.right_shift(position, bit_number), 1) == 1
        mixed = jnp.where(upper, partner - mixed, mixed + partner)
    return mixed


def body(tokens, clip_act, weight, clip_weight, cotangent):
    rotated = rotate(tokens.astype(jnp.float32))
    ratio_act = rotated / clip_act
    tanh_act = jnp.tanh(ratio_act)
    quant_act = (clip_act * tanh_act).astype(jnp.bfloat16)
    slope_act = 1.0 - tanh_act * tanh_act
    edge_act = tanh_act - ratio_act * slope_act
    all_act = lax.all_gather(quant_act, DP, axis=0, tiled=True)
    ratio_weight = weight.astype(jnp.float32) / clip_weight
    tanh_weight = jnp.tanh(ratio_weight)
    quant_weight = (clip_weight * tanh_weight).astype(jnp.bfloat16)
    block = all_act
    projected = lax.psum_scatter(
        jnp.dot(block, quant_weight, preferred_element_type=jnp.float32),
        "tensor",
        scatter_dimension=0,
        tiled=True,
    ).astype(jnp.bfloat16)
    all_cot = lax.all_gather(cotangent, "tensor", axis=0, tiled=True)
    weight_prod = lax.dot_general(
        all_act, all_cot, (((0,), (0,)), ((), ())), preferred_element_type=jnp.float32
    )
    slope_weight = 1.0 - tanh_weight * tanh_weight
    weight_grad = (weight_prod * slope_weight).astype(jnp.bfloat16)
    weight_terms = jnp.sum(weight_prod * (tanh_weight - ratio_weight * slope_weight), axis=0)
    clip_weight_grad = lax.psum(weight_terms, "tensor")
    block = all_cot
    act_prod = lax.psum_scatter(
        lax.dot_general(
            block, quant_weight, (((1,), (1,)), ((), ())), preferred_element_type=jnp.float32
        ).astype(jnp.bfloat16),
        DP,
        scatter_dimension=0,
        tiled=True,
    ).astype(jnp.float32)
    act_terms = jnp.sum(act_prod * edge_act, axis=0)
    for axis in ("dc", "dx", "dz"):
        act_terms = lax.psum(act_terms, axis)
    clip_act_grad = act_terms
    pre_rotation = act_prod * slope_act
    token_grad = rotate(pre_rotation).astype(jnp.bfloat16)
    return (projected, token_grad, weight_grad, clip_act_grad, clip_weight_grad)


DP = ("dx", "dz", "dc")


def solution(mesh):
    rows, cols = mesh.devices.shape
    cores = 2
    across = 4 if rows % (4 * cores) == 0 else 1
    grid = mesh.devices.reshape(across, rows // (across * cores), cores, cols)
    fine = jax.sharding.Mesh(grid, ("dx", "dz", "dc", "tensor"))
    in_specs = (P(DP, "tensor"), P("tensor"), P("tensor", DP), P(DP), P("tensor", DP))
    out_specs = (P("tensor", DP), P(DP, "tensor"), P("tensor", DP), P("tensor"), P(DP))
    return jax.shard_map(body, mesh=fine, in_specs=in_specs, out_specs=out_specs, check_vma=False)
```

```python
import math

import jax
import jax.numpy as jnp
from jax import lax
from jax.sharding import PartitionSpec as P


def swapped(block, axis, bit):
    count = lax.axis_size(axis)
    route = []
    for low in range(count):
        high = low | 1 << bit
        if high != low and high < count:
            route += [(low, high), (high, low)]
    return lax.ppermute(block, axis, route)


def sylvester(order):
    index = lax.iota(jnp.int32, order)
    joined = jnp.bitwise_and(index[:, None], index[None, :])
    parity = jnp.zeros((order, order), jnp.int32)
    for bit_number in range(max(order.bit_length() - 1, 0)):
        parity = parity + jnp.bitwise_and(jnp.right_shift(joined, bit_number), 1)
    return (1 - 2 * jnp.bitwise_and(parity, 1)).astype(jnp.float32)


def local_rotate(values, norm_factor):
    row_total, width = values.shape
    levels = width.bit_length() - 1
    outer = 2 ** (levels // 2)
    inner = width // outer
    blocks = values.reshape(row_total, outer, inner)
    blocks = jnp.einsum("rab,ac->rcb", blocks, sylvester(outer), precision=lax.Precision.HIGHEST)
    blocks = jnp.einsum("rcb,bd->rcd", blocks, sylvester(inner), precision=lax.Precision.HIGHEST)
    return blocks.reshape(row_total, width) * norm_factor


def rotate(values):
    group_size = lax.axis_size("tensor")
    norm_factor = 1.0 / math.sqrt(values.shape[1] * group_size)
    mixed = local_rotate(values, norm_factor)
    position = lax.axis_index("tensor")
    for bit_number in range(group_size.bit_length() - 1):
        partner = swapped(mixed, "tensor", bit_number)
        upper = jnp.bitwise_and(jnp.right_shift(position, bit_number), 1) == 1
        mixed = jnp.where(upper, partner - mixed, mixed + partner)
    return mixed


def body(tokens, clip_act, weight, clip_weight, cotangent):
    rotated = rotate(tokens.astype(jnp.float32))
    ratio_act = rotated / clip_act
    tanh_act = jnp.tanh(ratio_act)
    quant_act = (clip_act * tanh_act).astype(jnp.bfloat16)
    slope_act = 1.0 - tanh_act * tanh_act
    edge_act = tanh_act - ratio_act * slope_act
    rows, width = quant_act.shape
    chips = lax.axis_size("dx") * lax.axis_size("dz")
    cores = lax.axis_size("dc")
    core = lax.axis_index("dc")
    half_act = lax.all_gather(quant_act, CHIPS, axis=0, tiled=True)
    both_act = lax.all_gather(half_act, "dc", axis=0, tiled=False)
    all_act = (
        both_act.reshape(cores, chips, rows, width).transpose(1, 0, 2, 3).reshape(-1, width)
    )
    ratio_weight = weight.astype(jnp.float32) / clip_weight
    tanh_weight = jnp.tanh(ratio_weight)
    quant_weight = (clip_weight * tanh_weight).astype(jnp.bfloat16)
    block = all_act
    projected = lax.psum_scatter(
        jnp.dot(block, quant_weight, preferred_element_type=jnp.float32),
        "tensor",
        scatter_dimension=0,
        tiled=True,
    ).astype(jnp.bfloat16)
    all_cot = lax.all_gather(cotangent, "tensor", axis=0, tiled=True)
    weight_prod = lax.dot_general(
        all_act, all_cot, (((0,), (0,)), ((), ())), preferred_element_type=jnp.float32
    )
    slope_weight = 1.0 - tanh_weight * tanh_weight
    weight_grad = (weight_prod * slope_weight).astype(jnp.bfloat16)
    weight_terms = jnp.sum(weight_prod * (tanh_weight - ratio_weight * slope_weight), axis=0)
    clip_weight_grad = lax.psum(weight_terms, "tensor")
    block = all_cot
    partial = lax.dot_general(
        block, quant_weight, (((1,), (1,)), ((), ())), preferred_element_type=jnp.float32
    ).reshape(chips, cores, rows, width)
    mine = lax.dynamic_index_in_dim(partial, core, axis=1, keepdims=False)
    other = lax.dynamic_index_in_dim(partial, cores - 1 - core, axis=1, keepdims=False)
    pair = [(0, 1), (1, 0)]
    chip_sum = mine + lax.ppermute(other.astype(jnp.bfloat16), "dc", pair).astype(jnp.float32)
    pieces = lax.all_to_all(chip_sum.astype(jnp.bfloat16), CHIPS, 0, 0, tiled=True)
    act_prod = jnp.sum(pieces.astype(jnp.float32), axis=0)
    act_terms = lax.psum(jnp.sum(act_prod * edge_act, axis=0), "dc")
    clip_act_grad = jnp.sum(lax.all_gather(act_terms, CHIPS, axis=0, tiled=False), axis=0)
    pre_rotation = act_prod * slope_act
    token_grad = rotate(pre_rotation).astype(jnp.bfloat16)
    return (projected, token_grad, weight_grad, clip_act_grad, clip_weight_grad)


DP = ("dx", "dz", "dc")
CHIPS = ("dx", "dz")


def solution(mesh):
    rows, cols = mesh.devices.shape
    cores = 2
    across = 4 if rows % (4 * cores) == 0 else 1
    grid = mesh.devices.reshape(across, rows // (across * cores), cores, cols)
    fine = jax.sharding.Mesh(grid, ("dx", "dz", "dc", "tensor"))
    in_specs = (P(DP, "tensor"), P("tensor"), P("tensor", DP), P(DP), P("tensor", DP))
    out_specs = (P("tensor", DP), P(DP, "tensor"), P("tensor", DP), P("tensor"), P(DP))
    return jax.shard_map(body, mesh=fine, in_specs=in_specs, out_specs=out_specs, check_vma=False)
```

```python
import math

import jax
import jax.numpy as jnp
from jax import lax
from jax.sharding import PartitionSpec as P


def swapped(block, axis, bit):
    count = lax.axis_size(axis)
    route = []
    for low in range(count):
        high = low | 1 << bit
        if high != low and high < count:
            route += [(low, high), (high, low)]
    return lax.ppermute(block, axis, route)


def sylvester(order):
    index = lax.iota(jnp.int32, order)
    joined = jnp.bitwise_and(index[:, None], index[None, :])
    parity = jnp.zeros((order, order), jnp.int32)
    for bit_number in range(max(order.bit_length() - 1, 0)):
        parity = parity + jnp.bitwise_and(jnp.right_shift(joined, bit_number), 1)
    return (1 - 2 * jnp.bitwise_and(parity, 1)).astype(jnp.float32)


def local_rotate(values, norm_factor):
    row_total, width = values.shape
    levels = width.bit_length() - 1
    outer = 2 ** (levels // 2)
    inner = width // outer
    blocks = values.reshape(row_total, outer, inner)
    blocks = jnp.einsum("rab,ac->rcb", blocks, sylvester(outer), precision=lax.Precision.HIGHEST)
    blocks = jnp.einsum("rcb,bd->rcd", blocks, sylvester(inner), precision=lax.Precision.HIGHEST)
    return blocks.reshape(row_total, width) * norm_factor


def rotate(values):
    group_size = lax.axis_size("tensor")
    norm_factor = 1.0 / math.sqrt(values.shape[1] * group_size)
    mixed = local_rotate(values, norm_factor)
    position = lax.axis_index("tensor")
    for bit_number in range(group_size.bit_length() - 1):
        partner = swapped(mixed, "tensor", bit_number)
        upper = jnp.bitwise_and(jnp.right_shift(position, bit_number), 1) == 1
        mixed = jnp.where(upper, partner - mixed, mixed + partner)
    return mixed


def body(tokens, clip_act, weight, clip_weight, cotangent):
    rotated = rotate(tokens.astype(jnp.float32))
    ratio_act = rotated / clip_act
    tanh_act = jnp.tanh(ratio_act)
    quant_act = (clip_act * tanh_act).astype(jnp.bfloat16)
    slope_act = 1.0 - tanh_act * tanh_act
    edge_act = tanh_act - ratio_act * slope_act
    rows, width = quant_act.shape
    chips = lax.axis_size("dx") * lax.axis_size("dz")
    cores = lax.axis_size("dc")
    core = lax.axis_index("dc")
    ratio_weight = weight.astype(jnp.float32) / clip_weight
    tanh_weight = jnp.tanh(ratio_weight)
    quant_weight = (clip_weight * tanh_weight).astype(jnp.bfloat16)
    all_cot = lax.all_gather(cotangent, "tensor", axis=0, tiled=True)
    partial = lax.dot_general(
        all_cot, quant_weight, (((1,), (1,)), ((), ())), preferred_element_type=jnp.float32
    ).reshape(chips, cores, rows, width)
    quant_act, partial = lax.optimization_barrier((quant_act, partial))
    half_act = lax.all_gather(quant_act, CHIPS, axis=0, tiled=True)
    pair = [(0, 1), (1, 0)]
    partner_act = lax.ppermute(half_act, "dc", pair)
    both_act = jnp.where(
        core == 0, jnp.stack([half_act, partner_act]), jnp.stack([partner_act, half_act])
    )
    all_act = (
        both_act.reshape(cores, chips, rows, width).transpose(1, 0, 2, 3).reshape(-1, width)
    )
    block = all_act
    projected = lax.psum_scatter(
        jnp.dot(block, quant_weight, preferred_element_type=jnp.float32),
        "tensor",
        scatter_dimension=0,
        tiled=True,
    ).astype(jnp.bfloat16)
    weight_prod = lax.dot_general(
        all_act, all_cot, (((0,), (0,)), ((), ())), preferred_element_type=jnp.float32
    )
    slope_weight = 1.0 - tanh_weight * tanh_weight
    weight_grad = (weight_prod * slope_weight).astype(jnp.bfloat16)
    weight_terms = jnp.sum(weight_prod * (tanh_weight - ratio_weight * slope_weight), axis=0)
    clip_weight_grad = lax.psum(weight_terms, "tensor")
    mine = lax.dynamic_index_in_dim(partial, core, axis=1, keepdims=False)
    other = lax.dynamic_index_in_dim(partial, cores - 1 - core, axis=1, keepdims=False)
    chip_sum = mine + lax.ppermute(other.astype(jnp.bfloat16), "dc", pair).astype(jnp.float32)
    pieces = lax.all_to_all(chip_sum.astype(jnp.bfloat16), CHIPS, 0, 0, tiled=True)
    act_prod = jnp.sum(pieces.astype(jnp.float32), axis=0)
    act_terms = jnp.sum(act_prod * edge_act, axis=0)
    groups = lax.axis_size("tensor")
    slots = jnp.zeros((groups,) + act_terms.shape, act_terms.dtype)
    slots = lax.dynamic_update_index_in_dim(slots, act_terms, lax.axis_index("tensor"), 0)
    slots = lax.psum(slots, DP + ("tensor",))
    clip_act_grad = lax.dynamic_index_in_dim(slots, lax.axis_index("tensor"), 0, keepdims=False)
    pre_rotation = act_prod * slope_act
    token_grad = rotate(pre_rotation).astype(jnp.bfloat16)
    return (projected, token_grad, weight_grad, clip_act_grad, clip_weight_grad)


DP = ("dx", "dz", "dc")
CHIPS = ("dx", "dz")


def solution(mesh):
    rows, cols = mesh.devices.shape
    cores = 2
    across = 4 if rows % (4 * cores) == 0 else 1
    grid = mesh.devices.reshape(across, rows // (across * cores), cores, cols)
    fine = jax.sharding.Mesh(grid, ("dx", "dz", "dc", "tensor"))
    in_specs = (P(DP, "tensor"), P("tensor"), P("tensor", DP), P(DP), P("tensor", DP))
    out_specs = (P("tensor", DP), P(DP, "tensor"), P("tensor", DP), P("tensor"), P(DP))
    return jax.shard_map(body, mesh=fine, in_specs=in_specs, out_specs=out_specs, check_vma=False)
```

```python
import math

import jax
import jax.numpy as jnp
from jax import lax
from jax.sharding import PartitionSpec as P


def swapped(block, axis, bit):
    count = lax.axis_size(axis)
    route = []
    for low in range(count):
        high = low | 1 << bit
        if high != low and high < count:
            route += [(low, high), (high, low)]
    return lax.ppermute(block, axis, route)


def butterfly_sum(values, axis):
    for bit_number in range(lax.axis_size(axis).bit_length() - 1):
        values = values + swapped(values, axis, bit_number)
    return values


def sylvester(order):
    index = lax.iota(jnp.int32, order)
    joined = jnp.bitwise_and(index[:, None], index[None, :])
    parity = jnp.zeros((order, order), jnp.int32)
    for bit_number in range(max(order.bit_length() - 1, 0)):
        parity = parity + jnp.bitwise_and(jnp.right_shift(joined, bit_number), 1)
    return (1 - 2 * jnp.bitwise_and(parity, 1)).astype(jnp.float32)


def local_rotate(values, norm_factor):
    row_total, width = values.shape
    levels = width.bit_length() - 1
    outer = 2 ** (levels // 2)
    inner = width // outer
    blocks = values.reshape(row_total, outer, inner)
    blocks = jnp.einsum("rab,ac->rcb", blocks, sylvester(outer), precision=lax.Precision.HIGHEST)
    blocks = jnp.einsum("rcb,bd->rcd", blocks, sylvester(inner), precision=lax.Precision.HIGHEST)
    return blocks.reshape(row_total, width) * norm_factor


def rotate(values):
    group_size = lax.axis_size("tensor")
    norm_factor = 1.0 / math.sqrt(values.shape[1] * group_size)
    mixed = local_rotate(values, norm_factor)
    position = lax.axis_index("tensor")
    for bit_number in range(group_size.bit_length() - 1):
        partner = swapped(mixed, "tensor", bit_number)
        upper = jnp.bitwise_and(jnp.right_shift(position, bit_number), 1) == 1
        mixed = jnp.where(upper, partner - mixed, mixed + partner)
    return mixed


def body(tokens, clip_act, weight, clip_weight, cotangent):
    rotated = rotate(tokens.astype(jnp.float32))
    ratio_act = rotated / clip_act
    tanh_act = jnp.tanh(ratio_act)
    quant_act = (clip_act * tanh_act).astype(jnp.bfloat16)
    slope_act = 1.0 - tanh_act * tanh_act
    edge_act = tanh_act - ratio_act * slope_act
    rows, width = quant_act.shape
    chips = lax.axis_size("dx") * lax.axis_size("dz")
    cores = lax.axis_size("dc")
    core = lax.axis_index("dc")
    ratio_weight = weight.astype(jnp.float32) / clip_weight
    tanh_weight = jnp.tanh(ratio_weight)
    quant_weight = (clip_weight * tanh_weight).astype(jnp.bfloat16)
    all_cot = lax.all_gather(cotangent, "tensor", axis=0, tiled=True)
    partial = lax.dot_general(
        all_cot, quant_weight, (((1,), (1,)), ((), ())), preferred_element_type=jnp.float32
    ).reshape(chips, cores, rows, width)
    quant_act, partial = lax.optimization_barrier((quant_act, partial))
    half_act = lax.all_gather(quant_act, CHIPS, axis=0, tiled=True)
    pair = [(0, 1), (1, 0)]
    partner_act = lax.ppermute(half_act, "dc", pair)
    both_act = jnp.where(
        core == 0, jnp.stack([half_act, partner_act]), jnp.stack([partner_act, half_act])
    )
    all_act = (
        both_act.reshape(cores, chips, rows, width).transpose(1, 0, 2, 3).reshape(-1, width)
    )
    block = all_act
    projected = lax.psum_scatter(
        jnp.dot(block, quant_weight, preferred_element_type=jnp.float32),
        "tensor",
        scatter_dimension=0,
        tiled=True,
    ).astype(jnp.bfloat16)
    weight_prod = lax.dot_general(
        all_act, all_cot, (((0,), (0,)), ((), ())), preferred_element_type=jnp.float32
    )
    slope_weight = 1.0 - tanh_weight * tanh_weight
    weight_grad = (weight_prod * slope_weight).astype(jnp.bfloat16)
    weight_terms = jnp.sum(weight_prod * (tanh_weight - ratio_weight * slope_weight), axis=0)
    clip_weight_grad = butterfly_sum(weight_terms, "tensor")
    mine = lax.dynamic_index_in_dim(partial, core, axis=1, keepdims=False)
    other = lax.dynamic_index_in_dim(partial, cores - 1 - core, axis=1, keepdims=False)
    chip_sum = mine + lax.ppermute(other.astype(jnp.bfloat16), "dc", pair).astype(jnp.float32)
    pieces = lax.all_to_all(chip_sum.astype(jnp.bfloat16), CHIPS, 0, 0, tiled=True)
    act_prod = jnp.sum(pieces.astype(jnp.float32), axis=0)
    act_terms = jnp.sum(act_prod * edge_act, axis=0)
    for axis in DP:
        act_terms = butterfly_sum(act_terms, axis)
    clip_act_grad = act_terms
    pre_rotation = act_prod * slope_act
    token_grad = rotate(pre_rotation).astype(jnp.bfloat16)
    return (projected, token_grad, weight_grad, clip_act_grad, clip_weight_grad)


DP = ("dx", "dz", "dc")
CHIPS = ("dx", "dz")


def solution(mesh):
    rows, cols = mesh.devices.shape
    cores = 2
    across = 4 if rows % (4 * cores) == 0 else 1
    grid = mesh.devices.reshape(across, rows // (across * cores), cores, cols)
    fine = jax.sharding.Mesh(grid, ("dx", "dz", "dc", "tensor"))
    in_specs = (P(DP, "tensor"), P("tensor"), P("tensor", DP), P(DP), P("tensor", DP))
    out_specs = (P("tensor", DP), P(DP, "tensor"), P("tensor", DP), P("tensor"), P(DP))
    return jax.shard_map(body, mesh=fine, in_specs=in_specs, out_specs=out_specs, check_vma=False)
```

```python
import math

import jax
import jax.numpy as jnp
from jax import lax
from jax.sharding import PartitionSpec as P


def swapped(block, axis, bit):
    count = lax.axis_size(axis)
    route = []
    for low in range(count):
        high = low | 1 << bit
        if high != low and high < count:
            route += [(low, high), (high, low)]
    return lax.ppermute(block, axis, route)


def butterfly_sum(values, axis):
    for bit_number in range(lax.axis_size(axis).bit_length() - 1):
        values = values + swapped(values, axis, bit_number)
    return values


def sylvester(order):
    index = lax.iota(jnp.int32, order)
    joined = jnp.bitwise_and(index[:, None], index[None, :])
    parity = jnp.zeros((order, order), jnp.int32)
    for bit_number in range(max(order.bit_length() - 1, 0)):
        parity = parity + jnp.bitwise_and(jnp.right_shift(joined, bit_number), 1)
    return (1 - 2 * jnp.bitwise_and(parity, 1)).astype(jnp.float32)


def local_rotate(values, norm_factor):
    row_total, width = values.shape
    levels = width.bit_length() - 1
    outer = 2 ** (levels // 2)
    inner = width // outer
    blocks = values.reshape(row_total, outer, inner)
    blocks = jnp.einsum("rab,ac->rcb", blocks, sylvester(outer), precision=lax.Precision.HIGHEST)
    blocks = jnp.einsum("rcb,bd->rcd", blocks, sylvester(inner), precision=lax.Precision.HIGHEST)
    return blocks.reshape(row_total, width) * norm_factor


def rotate(values):
    group_size = lax.axis_size("tensor")
    norm_factor = 1.0 / math.sqrt(values.shape[1] * group_size)
    mixed = local_rotate(values, norm_factor)
    position = lax.axis_index("tensor")
    for bit_number in range(group_size.bit_length() - 1):
        partner = swapped(mixed, "tensor", bit_number)
        upper = jnp.bitwise_and(jnp.right_shift(position, bit_number), 1) == 1
        mixed = jnp.where(upper, partner - mixed, mixed + partner)
    return mixed


def body(tokens, clip_act, weight, clip_weight, cotangent):
    rotated = rotate(tokens.astype(jnp.float32))
    ratio_act = rotated / clip_act
    tanh_act = jnp.tanh(ratio_act)
    quant_act = (clip_act * tanh_act).astype(jnp.bfloat16)
    slope_act = 1.0 - tanh_act * tanh_act
    edge_act = tanh_act - ratio_act * slope_act
    rows, width = quant_act.shape
    chips = lax.axis_size("dx") * lax.axis_size("dz")
    cores = lax.axis_size("dc")
    core = lax.axis_index("dc")
    ratio_weight = weight.astype(jnp.float32) / clip_weight
    tanh_weight = jnp.tanh(ratio_weight)
    quant_weight = (clip_weight * tanh_weight).astype(jnp.bfloat16)
    all_cot = lax.all_gather(cotangent, "tensor", axis=0, tiled=True)
    partial = lax.dot_general(
        all_cot, quant_weight, (((1,), (1,)), ((), ())), preferred_element_type=jnp.float32
    ).reshape(chips, cores, rows, width)
    quant_act, partial = lax.optimization_barrier((quant_act, partial))
    half_act = lax.all_gather(quant_act, CHIPS, axis=0, tiled=True)
    pair = [(0, 1), (1, 0)]
    partner_act = lax.ppermute(half_act, "dc", pair)
    hidden = all_cot.shape[1]
    cot_split = all_cot.reshape(chips, cores, rows, hidden)
    cot_own = lax.dynamic_index_in_dim(cot_split, core, axis=1, keepdims=False)
    cot_partner = lax.dynamic_index_in_dim(cot_split, cores - 1 - core, axis=1, keepdims=False)
    proj_own = jnp.dot(half_act, quant_weight, preferred_element_type=jnp.float32)
    proj_partner = jnp.dot(partner_act, quant_weight, preferred_element_type=jnp.float32)
    proj_own = proj_own.reshape(chips, rows, hidden)
    proj_partner = proj_partner.reshape(chips, rows, hidden)
    proj_all = jnp.where(
        core == 0,
        jnp.stack([proj_own, proj_partner], axis=1),
        jnp.stack([proj_partner, proj_own], axis=1),
    ).reshape(-1, hidden)
    projected = lax.psum_scatter(
        proj_all, "tensor", scatter_dimension=0, tiled=True
    ).astype(jnp.bfloat16)
    contract = (((0,), (0,)), ((), ()))
    weight_prod = lax.dot_general(
        half_act, cot_own.reshape(-1, hidden), contract, preferred_element_type=jnp.float32
    ) + lax.dot_general(
        partner_act, cot_partner.reshape(-1, hidden), contract, preferred_element_type=jnp.float32
    )
    slope_weight = 1.0 - tanh_weight * tanh_weight
    weight_grad = (weight_prod * slope_weight).astype(jnp.bfloat16)
    weight_terms = jnp.sum(weight_prod * (tanh_weight - ratio_weight * slope_weight), axis=0)
    clip_weight_grad = butterfly_sum(weight_terms, "tensor")
    mine = lax.dynamic_index_in_dim(partial, core, axis=1, keepdims=False)
    other = lax.dynamic_index_in_dim(partial, cores - 1 - core, axis=1, keepdims=False)
    chip_sum = mine + lax.ppermute(other.astype(jnp.bfloat16), "dc", pair).astype(jnp.float32)
    pieces = lax.all_to_all(chip_sum.astype(jnp.bfloat16), CHIPS, 0, 0, tiled=True)
    act_prod = jnp.sum(pieces.astype(jnp.float32), axis=0)
    act_terms = jnp.sum(act_prod * edge_act, axis=0)
    for axis in DP:
        act_terms = butterfly_sum(act_terms, axis)
    clip_act_grad = act_terms
    pre_rotation = act_prod * slope_act
    token_grad = rotate(pre_rotation).astype(jnp.bfloat16)
    return (projected, token_grad, weight_grad, clip_act_grad, clip_weight_grad)


DP = ("dx", "dz", "dc")
CHIPS = ("dx", "dz")


def solution(mesh):
    rows, cols = mesh.devices.shape
    cores = 2
    across = 4 if rows % (4 * cores) == 0 else 1
    grid = mesh.devices.reshape(across, rows // (across * cores), cores, cols)
    fine = jax.sharding.Mesh(grid, ("dx", "dz", "dc", "tensor"))
    in_specs = (P(DP, "tensor"), P("tensor"), P("tensor", DP), P(DP), P("tensor", DP))
    out_specs = (P("tensor", DP), P(DP, "tensor"), P("tensor", DP), P("tensor"), P(DP))
    return jax.shard_map(body, mesh=fine, in_specs=in_specs, out_specs=out_specs, check_vma=False)
```

```python
import math

import jax
import jax.numpy as jnp
from jax import lax
from jax.sharding import PartitionSpec as P


def swapped(block, axis, bit):
    count = lax.axis_size(axis)
    route = []
    for low in range(count):
        high = low | 1 << bit
        if high != low and high < count:
            route += [(low, high), (high, low)]
    return lax.ppermute(block, axis, route)


def butterfly_sum(values, axis):
    for bit_number in range(lax.axis_size(axis).bit_length() - 1):
        values = values + swapped(values, axis, bit_number)
    return values


def sylvester(order):
    index = lax.iota(jnp.int32, order)
    joined = jnp.bitwise_and(index[:, None], index[None, :])
    parity = jnp.zeros((order, order), jnp.int32)
    for bit_number in range(max(order.bit_length() - 1, 0)):
        parity = parity + jnp.bitwise_and(jnp.right_shift(joined, bit_number), 1)
    return (1 - 2 * jnp.bitwise_and(parity, 1)).astype(jnp.float32)


def local_rotate(values, norm_factor):
    row_total, width = values.shape
    levels = width.bit_length() - 1
    outer = 2 ** (levels // 2)
    inner = width // outer
    blocks = values.reshape(row_total, outer, inner)
    blocks = jnp.einsum("rab,ac->rcb", blocks, sylvester(outer), precision=lax.Precision.HIGHEST)
    blocks = jnp.einsum("rcb,bd->rcd", blocks, sylvester(inner), precision=lax.Precision.HIGHEST)
    return blocks.reshape(row_total, width) * norm_factor


def rotate(values):
    group_size = lax.axis_size("tensor")
    norm_factor = 1.0 / math.sqrt(values.shape[1] * group_size)
    mixed = local_rotate(values, norm_factor)
    position = lax.axis_index("tensor")
    for bit_number in range(group_size.bit_length() - 1):
        partner = swapped(mixed, "tensor", bit_number)
        upper = jnp.bitwise_and(jnp.right_shift(position, bit_number), 1) == 1
        mixed = jnp.where(upper, partner - mixed, mixed + partner)
    return mixed


def body(tokens, clip_act, weight, clip_weight, cotangent):
    rotated = rotate(tokens.astype(jnp.float32))
    ratio_act = rotated / clip_act
    tanh_act = jnp.tanh(ratio_act)
    quant_act = (clip_act * tanh_act).astype(jnp.bfloat16)
    slope_act = 1.0 - tanh_act * tanh_act
    edge_act = tanh_act - ratio_act * slope_act
    rows, width = quant_act.shape
    chips = lax.axis_size("dx") * lax.axis_size("dz")
    cores = lax.axis_size("dc")
    core = lax.axis_index("dc")
    ratio_weight = weight.astype(jnp.float32) / clip_weight
    tanh_weight = jnp.tanh(ratio_weight)
    quant_weight = (clip_weight * tanh_weight).astype(jnp.bfloat16)
    all_cot = lax.all_gather(cotangent, "tensor", axis=0, tiled=True)
    partial = lax.dot_general(
        all_cot, quant_weight, (((1,), (1,)), ((), ())), preferred_element_type=jnp.float32
    ).reshape(chips, cores, rows, width)
    quant_act, partial = lax.optimization_barrier((quant_act, partial))
    all_act = lax.all_gather(quant_act, DP, axis=0, tiled=True)
    pair = [(0, 1), (1, 0)]
    block = all_act
    projected = lax.psum_scatter(
        jnp.dot(block, quant_weight, preferred_element_type=jnp.float32),
        "tensor",
        scatter_dimension=0,
        tiled=True,
    ).astype(jnp.bfloat16)
    weight_prod = lax.dot_general(
        all_act, all_cot, (((0,), (0,)), ((), ())), preferred_element_type=jnp.float32
    )
    slope_weight = 1.0 - tanh_weight * tanh_weight
    weight_grad = (weight_prod * slope_weight).astype(jnp.bfloat16)
    weight_terms = jnp.sum(weight_prod * (tanh_weight - ratio_weight * slope_weight), axis=0)
    clip_weight_grad = butterfly_sum(weight_terms, "tensor")
    mine = lax.dynamic_index_in_dim(partial, core, axis=1, keepdims=False)
    other = lax.dynamic_index_in_dim(partial, cores - 1 - core, axis=1, keepdims=False)
    chip_sum = mine + lax.ppermute(other.astype(jnp.bfloat16), "dc", pair).astype(jnp.float32)
    pieces = lax.all_to_all(chip_sum.astype(jnp.bfloat16), CHIPS, 0, 0, tiled=True)
    act_prod = jnp.sum(pieces.astype(jnp.float32), axis=0)
    act_terms = jnp.sum(act_prod * edge_act, axis=0)
    for axis in DP:
        act_terms = butterfly_sum(act_terms, axis)
    clip_act_grad = act_terms
    pre_rotation = act_prod * slope_act
    token_grad = rotate(pre_rotation).astype(jnp.bfloat16)
    return (projected, token_grad, weight_grad, clip_act_grad, clip_weight_grad)


DP = ("dx", "dz", "dc")
CHIPS = ("dx", "dz")


def solution(mesh):
    rows, cols = mesh.devices.shape
    cores = 2
    across = 4 if rows % (4 * cores) == 0 else 1
    grid = mesh.devices.reshape(across, rows // (across * cores), cores, cols)
    fine = jax.sharding.Mesh(grid, ("dx", "dz", "dc", "tensor"))
    in_specs = (P(DP, "tensor"), P("tensor"), P("tensor", DP), P(DP), P("tensor", DP))
    out_specs = (P("tensor", DP), P(DP, "tensor"), P("tensor", DP), P("tensor"), P(DP))
    return jax.shard_map(body, mesh=fine, in_specs=in_specs, out_specs=out_specs, check_vma=False)
```

```python
import math

import jax
import jax.numpy as jnp
from jax import lax
from jax.sharding import PartitionSpec as P


def swapped(block, axis, bit):
    count = lax.axis_size(axis)
    route = []
    for low in range(count):
        high = low | 1 << bit
        if high != low and high < count:
            route += [(low, high), (high, low)]
    return lax.ppermute(block, axis, route)


def butterfly_sum(values, axis):
    for bit_number in range(lax.axis_size(axis).bit_length() - 1):
        values = values + swapped(values, axis, bit_number)
    return values


def sylvester(order):
    index = lax.iota(jnp.int32, order)
    joined = jnp.bitwise_and(index[:, None], index[None, :])
    parity = jnp.zeros((order, order), jnp.int32)
    for bit_number in range(max(order.bit_length() - 1, 0)):
        parity = parity + jnp.bitwise_and(jnp.right_shift(joined, bit_number), 1)
    return (1 - 2 * jnp.bitwise_and(parity, 1)).astype(jnp.float32)


def local_rotate(values, norm_factor):
    row_total, width = values.shape
    levels = width.bit_length() - 1
    outer = 2 ** (levels // 2)
    inner = width // outer
    blocks = values.reshape(row_total, outer, inner)
    blocks = jnp.einsum("rab,ac->rcb", blocks, sylvester(outer), precision=lax.Precision.HIGHEST)
    blocks = jnp.einsum("rcb,bd->rcd", blocks, sylvester(inner), precision=lax.Precision.HIGHEST)
    return blocks.reshape(row_total, width) * norm_factor


def rotate(values):
    group_size = lax.axis_size("tensor")
    norm_factor = 1.0 / math.sqrt(values.shape[1] * group_size)
    mixed = local_rotate(values, norm_factor)
    position = lax.axis_index("tensor")
    for bit_number in range(group_size.bit_length() - 1):
        partner = swapped(mixed, "tensor", bit_number)
        upper = jnp.bitwise_and(jnp.right_shift(position, bit_number), 1) == 1
        mixed = jnp.where(upper, partner - mixed, mixed + partner)
    return mixed


def body(tokens, clip_act, weight, clip_weight, cotangent):
    rotated = rotate(tokens.astype(jnp.float32))
    ratio_act = rotated / clip_act
    tanh_act = jnp.tanh(ratio_act)
    quant_act = (clip_act * tanh_act).astype(jnp.bfloat16)
    slope_act = 1.0 - tanh_act * tanh_act
    edge_act = tanh_act - ratio_act * slope_act
    rows, width = quant_act.shape
    chips = lax.axis_size("dx") * lax.axis_size("dz")
    cores = lax.axis_size("dc")
    core = lax.axis_index("dc")
    ratio_weight = weight.astype(jnp.float32) / clip_weight
    tanh_weight = jnp.tanh(ratio_weight)
    quant_weight = (clip_weight * tanh_weight).astype(jnp.bfloat16)
    quant_act, quant_weight = lax.optimization_barrier((quant_act, quant_weight))
    all_act = lax.all_gather(quant_act, DP, axis=0, tiled=True)
    all_cot = lax.all_gather(cotangent, "tensor", axis=0, tiled=True)
    partial = lax.dot_general(
        all_cot, quant_weight, (((1,), (1,)), ((), ())), preferred_element_type=jnp.float32
    ).reshape(chips, cores, rows, width)
    pair = [(0, 1), (1, 0)]
    mine = lax.dynamic_index_in_dim(partial, core, axis=1, keepdims=False)
    other = lax.dynamic_index_in_dim(partial, cores - 1 - core, axis=1, keepdims=False)
    chip_sum = mine + lax.ppermute(other.astype(jnp.bfloat16), "dc", pair).astype(jnp.float32)
    pieces = lax.all_to_all(chip_sum.astype(jnp.bfloat16), CHIPS, 0, 0, tiled=True)
    all_act, pieces = lax.optimization_barrier((all_act, pieces))
    block = all_act
    proj_part = jnp.dot(block, quant_weight, preferred_element_type=jnp.float32)
    projected = lax.psum_scatter(
        proj_part,
        "tensor",
        scatter_dimension=0,
        tiled=True,
    ).astype(jnp.bfloat16)
    weight_prod = lax.dot_general(
        all_act, all_cot, (((0,), (0,)), ((), ())), preferred_element_type=jnp.float32
    )
    slope_weight = 1.0 - tanh_weight * tanh_weight
    weight_grad = (weight_prod * slope_weight).astype(jnp.bfloat16)
    weight_terms = jnp.sum(weight_prod * (tanh_weight - ratio_weight * slope_weight), axis=0)
    clip_weight_grad = butterfly_sum(weight_terms, "tensor")
    act_prod = jnp.sum(pieces.astype(jnp.float32), axis=0)
    act_terms = jnp.sum(act_prod * edge_act, axis=0)
    act_terms, _ = lax.optimization_barrier((act_terms, proj_part))
    for axis in DP:
        act_terms = butterfly_sum(act_terms, axis)
    clip_act_grad = act_terms
    pre_rotation = act_prod * slope_act
    token_grad = rotate(pre_rotation).astype(jnp.bfloat16)
    return (projected, token_grad, weight_grad, clip_act_grad, clip_weight_grad)


DP = ("dx", "dz", "dc")
CHIPS = ("dx", "dz")


def solution(mesh):
    rows, cols = mesh.devices.shape
    cores = 2
    across = 4 if rows % (4 * cores) == 0 else 1
    grid = mesh.devices.reshape(across, rows // (across * cores), cores, cols)
    fine = jax.sharding.Mesh(grid, ("dx", "dz", "dc", "tensor"))
    in_specs = (P(DP, "tensor"), P("tensor"), P("tensor", DP), P(DP), P("tensor", DP))
    out_specs = (P("tensor", DP), P(DP, "tensor"), P("tensor", DP), P("tensor"), P(DP))
    return jax.shard_map(body, mesh=fine, in_specs=in_specs, out_specs=out_specs, check_vma=False)
```

```python
import math

import jax
import jax.numpy as jnp
from jax import lax
from jax.sharding import PartitionSpec as P


def swapped(block, axis, bit):
    count = lax.axis_size(axis)
    route = []
    for low in range(count):
        high = low | 1 << bit
        if high != low and high < count:
            route += [(low, high), (high, low)]
    return lax.ppermute(block, axis, route)


def butterfly_sum(values, axis):
    for bit_number in range(lax.axis_size(axis).bit_length() - 1):
        values = values + swapped(values, axis, bit_number)
    return values


def sylvester(order):
    index = lax.iota(jnp.int32, order)
    joined = jnp.bitwise_and(index[:, None], index[None, :])
    parity = jnp.zeros((order, order), jnp.int32)
    for bit_number in range(max(order.bit_length() - 1, 0)):
        parity = parity + jnp.bitwise_and(jnp.right_shift(joined, bit_number), 1)
    return (1 - 2 * jnp.bitwise_and(parity, 1)).astype(jnp.float32)


def local_rotate(values, norm_factor):
    row_total, width = values.shape
    levels = width.bit_length() - 1
    outer = 2 ** (levels // 2)
    inner = width // outer
    blocks = values.reshape(row_total, outer, inner)
    blocks = jnp.einsum("rab,ac->rcb", blocks, sylvester(outer), precision=lax.Precision.HIGHEST)
    blocks = jnp.einsum("rcb,bd->rcd", blocks, sylvester(inner), precision=lax.Precision.HIGHEST)
    return blocks.reshape(row_total, width) * norm_factor


def rotate(values):
    group_size = lax.axis_size("tensor")
    norm_factor = 1.0 / math.sqrt(values.shape[1] * group_size)
    mixed = local_rotate(values, norm_factor)
    position = lax.axis_index("tensor")
    for bit_number in range(group_size.bit_length() - 1):
        partner = swapped(mixed, "tensor", bit_number)
        upper = jnp.bitwise_and(jnp.right_shift(position, bit_number), 1) == 1
        mixed = jnp.where(upper, partner - mixed, mixed + partner)
    return mixed


def body(tokens, clip_act, weight, clip_weight, cotangent):
    rotated = rotate(tokens.astype(jnp.float32))
    ratio_act = rotated / clip_act
    tanh_act = jnp.tanh(ratio_act)
    quant_act = (clip_act * tanh_act).astype(jnp.bfloat16)
    slope_act = 1.0 - tanh_act * tanh_act
    edge_act = tanh_act - ratio_act * slope_act
    rows, width = quant_act.shape
    chips = lax.axis_size("dx") * lax.axis_size("dz")
    cores = lax.axis_size("dc")
    core = lax.axis_index("dc")
    ratio_weight = weight.astype(jnp.float32) / clip_weight
    tanh_weight = jnp.tanh(ratio_weight)
    quant_weight = (clip_weight * tanh_weight).astype(jnp.bfloat16)
    quant_act, quant_weight = lax.optimization_barrier((quant_act, quant_weight))
    all_act = lax.all_gather(quant_act, DP, axis=0, tiled=True)
    all_cot = lax.all_gather(cotangent, "tensor", axis=0, tiled=True)
    partial = lax.dot_general(
        all_cot, quant_weight, (((1,), (1,)), ((), ())), preferred_element_type=jnp.float32
    ).reshape(chips, cores, rows, width)
    pair = [(0, 1), (1, 0)]
    mine = lax.dynamic_index_in_dim(partial, core, axis=1, keepdims=False)
    other = lax.dynamic_index_in_dim(partial, cores - 1 - core, axis=1, keepdims=False)
    chip_sum = mine + lax.ppermute(other.astype(jnp.bfloat16), "dc", pair).astype(jnp.float32)
    pieces = lax.all_to_all(chip_sum.astype(jnp.bfloat16), CHIPS, 0, 0, tiled=True)
    all_act, pieces = lax.optimization_barrier((all_act, pieces))
    block = all_act
    proj_part = jnp.dot(block, quant_weight, preferred_element_type=jnp.float32)
    projected = lax.psum_scatter(
        proj_part,
        "tensor",
        scatter_dimension=0,
        tiled=True,
    ).astype(jnp.bfloat16)
    weight_prod = lax.dot_general(
        all_act, all_cot, (((0,), (0,)), ((), ())), preferred_element_type=jnp.float32
    )
    slope_weight = 1.0 - tanh_weight * tanh_weight
    weight_grad = (weight_prod * slope_weight).astype(jnp.bfloat16)
    weight_terms = jnp.sum(weight_prod * (tanh_weight - ratio_weight * slope_weight), axis=0)
    act_prod = jnp.sum(pieces.astype(jnp.float32), axis=0)
    act_terms = jnp.sum(act_prod * edge_act, axis=0)
    act_terms, _, weight_terms = lax.optimization_barrier((act_terms, proj_part, weight_terms))
    for axis in DP:
        act_terms = butterfly_sum(act_terms, axis)
    clip_act_grad = act_terms
    clip_weight_grad = butterfly_sum(weight_terms, "tensor")
    pre_rotation = act_prod * slope_act
    token_grad = rotate(pre_rotation).astype(jnp.bfloat16)
    return (projected, token_grad, weight_grad, clip_act_grad, clip_weight_grad)


DP = ("dx", "dz", "dc")
CHIPS = ("dx", "dz")


def solution(mesh):
    rows, cols = mesh.devices.shape
    cores = 2
    across = 4 if rows % (4 * cores) == 0 else 1
    grid = mesh.devices.reshape(across, rows // (across * cores), cores, cols)
    fine = jax.sharding.Mesh(grid, ("dx", "dz", "dc", "tensor"))
    in_specs = (P(DP, "tensor"), P("tensor"), P("tensor", DP), P(DP), P("tensor", DP))
    out_specs = (P("tensor", DP), P(DP, "tensor"), P("tensor", DP), P("tensor"), P(DP))
    return jax.shard_map(body, mesh=fine, in_specs=in_specs, out_specs=out_specs, check_vma=False)
```

```python
import math

import jax
import jax.numpy as jnp
from jax import lax
from jax.sharding import PartitionSpec as P


def swapped(block, axis, bit):
    count = lax.axis_size(axis)
    route = []
    for low in range(count):
        high = low | 1 << bit
        if high != low and high < count:
            route += [(low, high), (high, low)]
    return lax.ppermute(block, axis, route)


def butterfly_sum(values, axis):
    for bit_number in range(lax.axis_size(axis).bit_length() - 1):
        values = values + swapped(values, axis, bit_number)
    return values


def sylvester(order):
    index = lax.iota(jnp.int32, order)
    joined = jnp.bitwise_and(index[:, None], index[None, :])
    parity = jnp.zeros((order, order), jnp.int32)
    for bit_number in range(max(order.bit_length() - 1, 0)):
        parity = parity + jnp.bitwise_and(jnp.right_shift(joined, bit_number), 1)
    return (1 - 2 * jnp.bitwise_and(parity, 1)).astype(jnp.float32)


def local_rotate(values, norm_factor):
    row_total, width = values.shape
    levels = width.bit_length() - 1
    outer = 2 ** (levels // 2)
    inner = width // outer
    blocks = values.reshape(row_total, outer, inner)
    blocks = jnp.einsum("rab,ac->rcb", blocks, sylvester(outer), precision=lax.Precision.HIGHEST)
    blocks = jnp.einsum("rcb,bd->rcd", blocks, sylvester(inner), precision=lax.Precision.HIGHEST)
    return blocks.reshape(row_total, width) * norm_factor


def rotate(values):
    group_size = lax.axis_size("tensor")
    norm_factor = 1.0 / math.sqrt(values.shape[1] * group_size)
    mixed = local_rotate(values, norm_factor)
    position = lax.axis_index("tensor")
    for bit_number in range(group_size.bit_length() - 1):
        partner = swapped(mixed, "tensor", bit_number)
        upper = jnp.bitwise_and(jnp.right_shift(position, bit_number), 1) == 1
        mixed = jnp.where(upper, partner - mixed, mixed + partner)
    return mixed


def body(tokens, clip_act, weight, clip_weight, cotangent):
    rotated = rotate(tokens.astype(jnp.float32))
    ratio_act = rotated / clip_act
    tanh_act = jnp.tanh(ratio_act)
    quant_act = (clip_act * tanh_act).astype(jnp.bfloat16)
    slope_act = 1.0 - tanh_act * tanh_act
    edge_act = tanh_act - ratio_act * slope_act
    rows, width = quant_act.shape
    chips = lax.axis_size("dx") * lax.axis_size("dz")
    cores = lax.axis_size("dc")
    core = lax.axis_index("dc")
    ratio_weight = weight.astype(jnp.float32) / clip_weight
    tanh_weight = jnp.tanh(ratio_weight)
    quant_weight = (clip_weight * tanh_weight).astype(jnp.bfloat16)
    all_cot = lax.all_gather(cotangent, "tensor", axis=0, tiled=True)
    partial = lax.dot_general(
        all_cot, quant_weight, (((1,), (1,)), ((), ())), preferred_element_type=jnp.float32
    ).reshape(chips, cores, rows, width)
    quant_act, partial = lax.optimization_barrier((quant_act, partial))
    all_act = lax.all_gather(quant_act, DP, axis=0, tiled=True)
    pair = [(0, 1), (1, 0)]
    block = all_act
    projected = lax.psum_scatter(
        jnp.dot(block, quant_weight, preferred_element_type=jnp.float32),
        "tensor",
        scatter_dimension=0,
        tiled=True,
    ).astype(jnp.bfloat16)
    weight_prod = lax.dot_general(
        all_act, all_cot, (((0,), (0,)), ((), ())), preferred_element_type=jnp.float32
    )
    slope_weight = 1.0 - tanh_weight * tanh_weight
    weight_grad = (weight_prod * slope_weight).astype(jnp.bfloat16)
    weight_terms = jnp.sum(weight_prod * (tanh_weight - ratio_weight * slope_weight), axis=0)
    clip_weight_grad = butterfly_sum(weight_terms, "tensor")
    mine = lax.dynamic_index_in_dim(partial, core, axis=1, keepdims=False)
    other = lax.dynamic_index_in_dim(partial, cores - 1 - core, axis=1, keepdims=False)
    chip_sum = mine + lax.ppermute(other.astype(jnp.bfloat16), "dc", pair).astype(jnp.float32)
    pieces = lax.all_to_all(chip_sum.astype(jnp.bfloat16), CHIPS, 0, 0, tiled=True)
    act_prod = jnp.sum(pieces.astype(jnp.float32), axis=0)
    act_terms = jnp.sum(act_prod * edge_act, axis=0)
    act_terms = lax.psum(act_terms, "dc")
    spread = jnp.broadcast_to(act_terms[None], (chips,) + act_terms.shape)
    clip_act_grad = jnp.sum(lax.all_to_all(spread, CHIPS, 0, 0, tiled=True), axis=0)
    pre_rotation = act_prod * slope_act
    token_grad = rotate(pre_rotation).astype(jnp.bfloat16)
    return (projected, token_grad, weight_grad, clip_act_grad, clip_weight_grad)


DP = ("dx", "dz", "dc")
CHIPS = ("dx", "dz")


def solution(mesh):
    rows, cols = mesh.devices.shape
    cores = 2
    across = 4 if rows % (4 * cores) == 0 else 1
    grid = mesh.devices.reshape(across, rows // (across * cores), cores, cols)
    fine = jax.sharding.Mesh(grid, ("dx", "dz", "dc", "tensor"))
    in_specs = (P(DP, "tensor"), P("tensor"), P("tensor", DP), P(DP), P("tensor", DP))
    out_specs = (P("tensor", DP), P(DP, "tensor"), P("tensor", DP), P("tensor"), P(DP))
    return jax.shard_map(body, mesh=fine, in_specs=in_specs, out_specs=out_specs, check_vma=False)
```

```python
import math

import jax
import jax.numpy as jnp
from jax import lax
from jax.sharding import PartitionSpec as P


def swapped(block, axis, bit):
    count = lax.axis_size(axis)
    route = []
    for low in range(count):
        high = low | 1 << bit
        if high != low and high < count:
            route += [(low, high), (high, low)]
    return lax.ppermute(block, axis, route)


def butterfly_sum(values, axis):
    for bit_number in range(lax.axis_size(axis).bit_length() - 1):
        values = values + swapped(values, axis, bit_number)
    return values


def sylvester(order):
    index = lax.iota(jnp.int32, order)
    joined = jnp.bitwise_and(index[:, None], index[None, :])
    parity = jnp.zeros((order, order), jnp.int32)
    for bit_number in range(max(order.bit_length() - 1, 0)):
        parity = parity + jnp.bitwise_and(jnp.right_shift(joined, bit_number), 1)
    return (1 - 2 * jnp.bitwise_and(parity, 1)).astype(jnp.float32)


def local_rotate(values, norm_factor):
    row_total, width = values.shape
    levels = width.bit_length() - 1
    outer = 2 ** (levels // 2)
    inner = width // outer
    blocks = values.reshape(row_total, outer, inner)
    blocks = jnp.einsum("rab,ac->rcb", blocks, sylvester(outer), precision=lax.Precision.HIGHEST)
    blocks = jnp.einsum("rcb,bd->rcd", blocks, sylvester(inner), precision=lax.Precision.HIGHEST)
    return blocks.reshape(row_total, width) * norm_factor


def rotate(values):
    group_size = lax.axis_size("tensor")
    norm_factor = 1.0 / math.sqrt(values.shape[1] * group_size)
    mixed = local_rotate(values, norm_factor)
    position = lax.axis_index("tensor")
    for bit_number in range(group_size.bit_length() - 1):
        partner = swapped(mixed, "tensor", bit_number)
        upper = jnp.bitwise_and(jnp.right_shift(position, bit_number), 1) == 1
        mixed = jnp.where(upper, partner - mixed, mixed + partner)
    return mixed


def body(tokens, clip_act, weight, clip_weight, cotangent):
    rotated = rotate(tokens.astype(jnp.float32))
    ratio_act = rotated / clip_act
    tanh_act = jnp.tanh(ratio_act)
    quant_act = (clip_act * tanh_act).astype(jnp.bfloat16)
    slope_act = 1.0 - tanh_act * tanh_act
    edge_act = tanh_act - ratio_act * slope_act
    rows, width = quant_act.shape
    chips = lax.axis_size("dx") * lax.axis_size("dz")
    cores = lax.axis_size("dc")
    core = lax.axis_index("dc")
    ratio_weight = weight.astype(jnp.float32) / clip_weight
    tanh_weight = jnp.tanh(ratio_weight)
    quant_weight = (clip_weight * tanh_weight).astype(jnp.bfloat16)
    all_cot = lax.all_gather(cotangent, "tensor", axis=0, tiled=True)
    partial = lax.dot_general(
        all_cot, quant_weight, (((1,), (1,)), ((), ())), preferred_element_type=jnp.float32
    ).reshape(chips, cores, rows, width)
    quant_act, partial = lax.optimization_barrier((quant_act, partial))
    all_act = lax.all_gather(quant_act, DP, axis=0, tiled=True)
    pair = [(0, 1), (1, 0)]
    block = all_act
    proj_part = jnp.dot(block, quant_weight, preferred_element_type=jnp.float32)
    projected = lax.psum_scatter(
        proj_part,
        "tensor",
        scatter_dimension=0,
        tiled=True,
    ).astype(jnp.bfloat16)
    weight_prod = lax.dot_general(
        all_act, all_cot, (((0,), (0,)), ((), ())), preferred_element_type=jnp.float32
    )
    slope_weight = 1.0 - tanh_weight * tanh_weight
    weight_grad = (weight_prod * slope_weight).astype(jnp.bfloat16)
    weight_terms = jnp.sum(weight_prod * (tanh_weight - ratio_weight * slope_weight), axis=0)
    clip_weight_grad = butterfly_sum(weight_terms, "tensor")
    mine = lax.dynamic_index_in_dim(partial, core, axis=1, keepdims=False)
    other = lax.dynamic_index_in_dim(partial, cores - 1 - core, axis=1, keepdims=False)
    chip_sum = mine + lax.ppermute(other.astype(jnp.bfloat16), "dc", pair).astype(jnp.float32)
    pieces = lax.all_to_all(chip_sum.astype(jnp.bfloat16), CHIPS, 0, 0, tiled=True)
    act_prod = jnp.sum(pieces.astype(jnp.float32), axis=0)
    act_terms = jnp.sum(act_prod * edge_act, axis=0)
    act_terms, _ = lax.optimization_barrier((act_terms, proj_part))
    act_terms = lax.psum(act_terms, "dc")
    spread = jnp.broadcast_to(act_terms[None], (chips,) + act_terms.shape)
    clip_act_grad = jnp.sum(lax.all_to_all(spread, CHIPS, 0, 0, tiled=True), axis=0)
    pre_rotation = act_prod * slope_act
    token_grad = rotate(pre_rotation).astype(jnp.bfloat16)
    return (projected, token_grad, weight_grad, clip_act_grad, clip_weight_grad)


DP = ("dx", "dz", "dc")
CHIPS = ("dx", "dz")


def solution(mesh):
    rows, cols = mesh.devices.shape
    cores = 2
    across = 4 if rows % (4 * cores) == 0 else 1
    grid = mesh.devices.reshape(across, rows // (across * cores), cores, cols)
    fine = jax.sharding.Mesh(grid, ("dx", "dz", "dc", "tensor"))
    in_specs = (P(DP, "tensor"), P("tensor"), P("tensor", DP), P(DP), P("tensor", DP))
    out_specs = (P("tensor", DP), P(DP, "tensor"), P("tensor", DP), P("tensor"), P(DP))
    return jax.shard_map(body, mesh=fine, in_specs=in_specs, out_specs=out_specs, check_vma=False)
```

```python
import math

import jax
import jax.numpy as jnp
from jax import lax
from jax.sharding import PartitionSpec as P


def swapped(block, axis, bit):
    count = lax.axis_size(axis)
    route = []
    for low in range(count):
        high = low | 1 << bit
        if high != low and high < count:
            route += [(low, high), (high, low)]
    return lax.ppermute(block, axis, route)


def butterfly_sum(values, axis):
    for bit_number in range(lax.axis_size(axis).bit_length() - 1):
        values = values + swapped(values, axis, bit_number)
    return values


def sylvester(order):
    index = lax.iota(jnp.int32, order)
    joined = jnp.bitwise_and(index[:, None], index[None, :])
    parity = jnp.zeros((order, order), jnp.int32)
    for bit_number in range(max(order.bit_length() - 1, 0)):
        parity = parity + jnp.bitwise_and(jnp.right_shift(joined, bit_number), 1)
    return (1 - 2 * jnp.bitwise_and(parity, 1)).astype(jnp.float32)


def local_rotate(values, norm_factor):
    row_total, width = values.shape
    levels = width.bit_length() - 1
    outer = 2 ** (levels // 2)
    inner = width // outer
    blocks = values.reshape(row_total, outer, inner)
    blocks = jnp.einsum("rab,ac->rcb", blocks, sylvester(outer), precision=lax.Precision.HIGHEST)
    blocks = jnp.einsum("rcb,bd->rcd", blocks, sylvester(inner), precision=lax.Precision.HIGHEST)
    return blocks.reshape(row_total, width) * norm_factor


def rotate(values):
    group_size = lax.axis_size("tensor")
    norm_factor = 1.0 / math.sqrt(values.shape[1] * group_size)
    mixed = local_rotate(values, norm_factor)
    position = lax.axis_index("tensor")
    for bit_number in range(group_size.bit_length() - 1):
        partner = swapped(mixed, "tensor", bit_number)
        upper = jnp.bitwise_and(jnp.right_shift(position, bit_number), 1) == 1
        mixed = jnp.where(upper, partner - mixed, mixed + partner)
    return mixed


def body(tokens, clip_act, weight, clip_weight, cotangent):
    rotated = rotate(tokens.astype(jnp.float32))
    ratio_act = rotated / clip_act
    tanh_act = jnp.tanh(ratio_act)
    quant_act = (clip_act * tanh_act).astype(jnp.bfloat16)
    slope_act = 1.0 - tanh_act * tanh_act
    edge_act = tanh_act - ratio_act * slope_act
    rows, width = quant_act.shape
    chips = lax.axis_size("dx") * lax.axis_size("dz")
    cores = lax.axis_size("dc")
    core = lax.axis_index("dc")
    ratio_weight = weight.astype(jnp.float32) / clip_weight
    tanh_weight = jnp.tanh(ratio_weight)
    quant_weight = (clip_weight * tanh_weight).astype(jnp.bfloat16)
    all_cot = cotangent
    position = lax.axis_index("tensor")
    for bit_number in range(lax.axis_size("tensor").bit_length() - 1):
        partner = swapped(all_cot, "tensor", bit_number)
        upper = jnp.bitwise_and(jnp.right_shift(position, bit_number), 1) == 1
        all_cot = jnp.where(
            upper,
            jnp.concatenate([partner, all_cot]),
            jnp.concatenate([all_cot, partner]),
        )
    partial = lax.dot_general(
        all_cot, quant_weight, (((1,), (1,)), ((), ())), preferred_element_type=jnp.float32
    ).reshape(chips, cores, rows, width)
    quant_act, partial = lax.optimization_barrier((quant_act, partial))
    all_act = lax.all_gather(quant_act, DP, axis=0, tiled=True)
    pair = [(0, 1), (1, 0)]
    block = all_act
    projected = lax.psum_scatter(
        jnp.dot(block, quant_weight, preferred_element_type=jnp.float32),
        "tensor",
        scatter_dimension=0,
        tiled=True,
    ).astype(jnp.bfloat16)
    weight_prod = lax.dot_general(
        all_act, all_cot, (((0,), (0,)), ((), ())), preferred_element_type=jnp.float32
    )
    slope_weight = 1.0 - tanh_weight * tanh_weight
    weight_grad = (weight_prod * slope_weight).astype(jnp.bfloat16)
    weight_terms = jnp.sum(weight_prod * (tanh_weight - ratio_weight * slope_weight), axis=0)
    clip_weight_grad = butterfly_sum(weight_terms, "tensor")
    mine = lax.dynamic_index_in_dim(partial, core, axis=1, keepdims=False)
    other = lax.dynamic_index_in_dim(partial, cores - 1 - core, axis=1, keepdims=False)
    chip_sum = mine + lax.ppermute(other.astype(jnp.bfloat16), "dc", pair).astype(jnp.float32)
    pieces = lax.all_to_all(chip_sum.astype(jnp.bfloat16), CHIPS, 0, 0, tiled=True)
    act_prod = jnp.sum(pieces.astype(jnp.float32), axis=0)
    act_terms = jnp.sum(act_prod * edge_act, axis=0)
    act_terms = lax.psum(act_terms, "dc")
    spread = jnp.broadcast_to(act_terms[None], (chips,) + act_terms.shape)
    clip_act_grad = jnp.sum(lax.all_to_all(spread, CHIPS, 0, 0, tiled=True), axis=0)
    pre_rotation = act_prod * slope_act
    token_grad = rotate(pre_rotation).astype(jnp.bfloat16)
    return (projected, token_grad, weight_grad, clip_act_grad, clip_weight_grad)


DP = ("dx", "dz", "dc")
CHIPS = ("dx", "dz")


def solution(mesh):
    rows, cols = mesh.devices.shape
    cores = 2
    across = 4 if rows % (4 * cores) == 0 else 1
    grid = mesh.devices.reshape(across, rows // (across * cores), cores, cols)
    fine = jax.sharding.Mesh(grid, ("dx", "dz", "dc", "tensor"))
    in_specs = (P(DP, "tensor"), P("tensor"), P("tensor", DP), P(DP), P("tensor", DP))
    out_specs = (P("tensor", DP), P(DP, "tensor"), P("tensor", DP), P("tensor"), P(DP))
    return jax.shard_map(body, mesh=fine, in_specs=in_specs, out_specs=out_specs, check_vma=False)
```

```python
import math

import jax
import jax.numpy as jnp
from jax import lax
from jax.sharding import PartitionSpec as P


def swapped(block, axis, bit):
    count = lax.axis_size(axis)
    route = []
    for low in range(count):
        high = low | 1 << bit
        if high != low and high < count:
            route += [(low, high), (high, low)]
    return lax.ppermute(block, axis, route)


def butterfly_sum(values, axis):
    for bit_number in range(lax.axis_size(axis).bit_length() - 1):
        values = values + swapped(values, axis, bit_number)
    return values


def sylvester(order):
    index = lax.iota(jnp.int32, order)
    joined = jnp.bitwise_and(index[:, None], index[None, :])
    parity = jnp.zeros((order, order), jnp.int32)
    for bit_number in range(max(order.bit_length() - 1, 0)):
        parity = parity + jnp.bitwise_and(jnp.right_shift(joined, bit_number), 1)
    return (1 - 2 * jnp.bitwise_and(parity, 1)).astype(jnp.float32)


def local_rotate(values, norm_factor):
    row_total, width = values.shape
    levels = width.bit_length() - 1
    outer = 2 ** (levels // 2)
    inner = width // outer
    blocks = values.reshape(row_total, outer, inner)
    blocks = jnp.einsum("rab,ac->rcb", blocks, sylvester(outer), precision=lax.Precision.HIGHEST)
    blocks = jnp.einsum("rcb,bd->rcd", blocks, sylvester(inner), precision=lax.Precision.HIGHEST)
    return blocks.reshape(row_total, width) * norm_factor


def rotate(values):
    group_size = lax.axis_size("tensor")
    norm_factor = 1.0 / math.sqrt(values.shape[1] * group_size)
    mixed = local_rotate(values, norm_factor)
    position = lax.axis_index("tensor")
    for bit_number in range(group_size.bit_length() - 1):
        partner = swapped(mixed, "tensor", bit_number)
        upper = jnp.bitwise_and(jnp.right_shift(position, bit_number), 1) == 1
        mixed = jnp.where(upper, partner - mixed, mixed + partner)
    return mixed


def body(tokens, clip_act, weight, clip_weight, cotangent):
    rotated = rotate(tokens.astype(jnp.float32))
    ratio_act = rotated / clip_act
    tanh_act = jnp.tanh(ratio_act)
    quant_act = (clip_act * tanh_act).astype(jnp.bfloat16)
    slope_act = 1.0 - tanh_act * tanh_act
    edge_act = tanh_act - ratio_act * slope_act
    rows, width = quant_act.shape
    chips = lax.axis_size("dx") * lax.axis_size("dz")
    cores = lax.axis_size("dc")
    core = lax.axis_index("dc")
    ratio_weight = weight.astype(jnp.float32) / clip_weight
    tanh_weight = jnp.tanh(ratio_weight)
    quant_weight = (clip_weight * tanh_weight).astype(jnp.bfloat16)
    all_cot = lax.all_gather(cotangent, "tensor", axis=0, tiled=True)
    partial = lax.dot_general(
        all_cot, quant_weight, (((1,), (1,)), ((), ())), preferred_element_type=jnp.float32
    ).reshape(chips, cores, rows, width)
    quant_act, partial = lax.optimization_barrier((quant_act, partial))
    all_act = lax.all_gather(quant_act, DP, axis=0, tiled=True)
    pair = [(0, 1), (1, 0)]
    block = all_act
    proj_part = jnp.dot(block, quant_weight, preferred_element_type=jnp.float32)
    proj_pieces = proj_part.reshape((lax.axis_size("tensor"), -1) + proj_part.shape[1:])
    proj_pieces = lax.all_to_all(proj_pieces.astype(jnp.bfloat16), "tensor", 0, 0, tiled=True)
    projected = jnp.sum(proj_pieces.astype(jnp.float32), axis=0).astype(jnp.bfloat16)
    weight_prod = lax.dot_general(
        all_act, all_cot, (((0,), (0,)), ((), ())), preferred_element_type=jnp.float32
    )
    slope_weight = 1.0 - tanh_weight * tanh_weight
    weight_grad = (weight_prod * slope_weight).astype(jnp.bfloat16)
    weight_terms = jnp.sum(weight_prod * (tanh_weight - ratio_weight * slope_weight), axis=0)
    clip_weight_grad = butterfly_sum(weight_terms, "tensor")
    mine = lax.dynamic_index_in_dim(partial, core, axis=1, keepdims=False)
    other = lax.dynamic_index_in_dim(partial, cores - 1 - core, axis=1, keepdims=False)
    chip_sum = mine + lax.ppermute(other.astype(jnp.bfloat16), "dc", pair).astype(jnp.float32)
    pieces = lax.all_to_all(chip_sum.astype(jnp.bfloat16), CHIPS, 0, 0, tiled=True)
    act_prod = jnp.sum(pieces.astype(jnp.float32), axis=0)
    act_terms = jnp.sum(act_prod * edge_act, axis=0)
    act_terms = lax.psum(act_terms, "dc")
    spread = jnp.broadcast_to(act_terms[None], (chips,) + act_terms.shape)
    clip_act_grad = jnp.sum(lax.all_to_all(spread, CHIPS, 0, 0, tiled=True), axis=0)
    pre_rotation = act_prod * slope_act
    token_grad = rotate(pre_rotation).astype(jnp.bfloat16)
    return (projected, token_grad, weight_grad, clip_act_grad, clip_weight_grad)


DP = ("dx", "dz", "dc")
CHIPS = ("dx", "dz")


def solution(mesh):
    rows, cols = mesh.devices.shape
    cores = 2
    across = 4 if rows % (4 * cores) == 0 else 1
    grid = mesh.devices.reshape(across, rows // (across * cores), cores, cols)
    fine = jax.sharding.Mesh(grid, ("dx", "dz", "dc", "tensor"))
    in_specs = (P(DP, "tensor"), P("tensor"), P("tensor", DP), P(DP), P("tensor", DP))
    out_specs = (P("tensor", DP), P(DP, "tensor"), P("tensor", DP), P("tensor"), P(DP))
    return jax.shard_map(body, mesh=fine, in_specs=in_specs, out_specs=out_specs, check_vma=False)
```
